512 devices in a mesh: gx: 16 (over y_lo, z), gy: 8 (over y_hi, core), rep: 4 (over x).
Axes of the slice: x: 4, y: 8 (y_hi: 4, y_lo: 2; y = y_hi * 2 + y_lo), z: 8, core: 2. Of those that a mesh axis runs over, the one named last changes fastest.
Arguments:
- positions: float32 [4, 3, 256, 16384], P('rep', None, 'gx', 'gy'), may hold values from 0 to 4
- velocities: float32 [4, 3, 256, 16384], P('rep', None, 'gx', 'gy'), may hold values from -6 to 6
- noise: float32 [4, 3, 256, 16384], P('rep', None, 'gx', 'gy'), may hold values from -6 to 6
- bonds: int32 [256, 256, 8], P('gx', 'gy'), may hold values from 0 to 1, as said below
Outputs:
- mean_force: float32 [3, 256, 16384], P(None, 'gx', 'gy')
- new_velocity: float32 [4, 3, 256, 16384], P('rep', None, 'gx', 'gy')
- new_position: float32 [4, 3, 256, 16384], P('rep', None, 'gx', 'gy')
The draws below stay inside these ranges and needn't reach their ends.
Inputs may be any that keep to these rules, and one draw needn't show every extreme that they name: bonds is symmetric: bonds of cluster c for offset k equals bonds of cluster c + offset k for the opposite offset k + 4 (k < 4); entries for neighbours outside the grid are 0.
All inputs are finite; a program needn't handle non-finite values.
Results may differ from the reference program's by a relative error of at most 0.0001.
Values sent between devices are 32-bit elements; how exact they have to be, the bound alone decides.
No kernel may reach another device: no remote copies, remote signals or barrier semaphores. Data moves between devices by JAX's collectives and lax.ppermute only.
A program may use at most 64 MiB of HBM per device.

```python
import jax
import jax.numpy as jnp
from jax import lax

ATOMS = 64
NXC = 256
NYC = 256
REPS = 4
N_REP = 4


half_offsets = ((0, 1), (1, -1), (1, 0), (1, 1))


def draw_bonds(key, part):
    half_flags = (jax.random.randint(key, (NXC, NYC, 4), 0, 4) < 3).astype(jnp.int32)
    row_ids = jnp.arange(NXC, dtype=jnp.int32)[:, None]
    col_ids = jnp.arange(NYC, dtype=jnp.int32)[None, :]
    forward = []
    for offset_index in range(4):
        shift_x, shift_y = half_offsets[offset_index]
        inside = (row_ids + shift_x >= 0) & (row_ids + shift_x < NXC) & (col_ids + shift_y >= 0) & (col_ids + shift_y < NYC)
        forward.append(half_flags[:, :, offset_index] * inside.astype(jnp.int32))
    forward_flags = jnp.stack(forward, axis=-1)
    padded = jnp.pad(forward_flags, ((1, 1), (1, 1), (0, 0)))
    backward = []
    for offset_index in range(4):
        shift_x, shift_y = half_offsets[offset_index]
        backward.append(padded[1 - shift_x:1 - shift_x + NXC, 1 - shift_y:1 - shift_y + NYC, offset_index])
    return jnp.concatenate([forward_flags, jnp.stack(backward, axis=-1)], axis=-1).astype(jnp.int32)


def levels(rng, shape, pieces, smallest, largest):
    gain, own = 1.0, jax.random.fold_in(rng, 6)
    for axis_at, blocks in pieces:
        heights = jnp.exp(jax.random.uniform(jax.random.fold_in(own, axis_at), (blocks,), jnp.float32, smallest / len(pieces), largest / len(pieces)))
        gain = gain * jnp.repeat(heights, shape[axis_at] // blocks).reshape([-1 if axis == axis_at else 1 for axis in range(len(shape))])
    return gain


def bell_draw(key, dims, spread, limit, cuts=(), kind=jnp.bfloat16):
    values = jax.random.normal(key, dims, jnp.float32) * spread
    if len(cuts) > 0:
        values = levels(key, dims, cuts, -0.22, 0.18) * values
    return jnp.clip(values, min=-limit, max=limit).astype(kind)


def setup_inputs(seed: int = 0) -> dict:
    splits = jax.random.split(jax.random.key(seed), 5)
    return {
        "positions": jnp.clip(4.0 * jax.random.uniform(splits[0], (REPS, 3, NXC, NYC * ATOMS), jnp.float32) ** levels(splits[0], (REPS, 3, NXC, NYC * ATOMS), ((0, 4), (2, 16), (3, 8)), -0.2, 0.2), 0.0, 4.0),
        "velocities": bell_draw(splits[1], (REPS, 3, NXC, NYC * ATOMS), 1.0, 6.0, ((0, 4), (2, 16), (3, 8)), jnp.float32),
        "noise": bell_draw(splits[2], (REPS, 3, NXC, NYC * ATOMS), 1.0, 6.0, ((0, 4), (2, 16), (3, 8)), jnp.float32),
        "bonds": draw_bonds(jax.random.fold_in(splits[4], 71), 0),
    }


spacing = 4.0
friction = 0.6
noise_coef = 0.8
time_step = 0.2
offsets_list = ((0, 1), (1, -1), (1, 0), (1, 1), (0, -1), (-1, 1), (-1, 0), (-1, -1))


def pair_weight(squared):
    return 2.0 * jnp.exp(-2.0 * squared) - 0.5 * jnp.exp(-0.5 * squared)


def tile_forces(own_atoms, neighbour, flag_col, shift_x, shift_y):
    shift_vec = jnp.array([shift_x * spacing, shift_y * spacing, 0.0], jnp.float32)[:, None, None]
    moved_atoms = neighbour + shift_vec
    differ = own_atoms[:, :, :, None] - moved_atoms[:, :, None, :]
    squared = jnp.sum(differ * differ, axis=0)
    weighted = (pair_weight(squared) * flag_col[:, None, None])[None] * differ
    return jnp.sum(weighted, axis=3), -jnp.sum(weighted, axis=2)


def reference(positions, velocities, noise, bonds):
    rows_total = positions.shape[2]
    cols_total = positions.shape[3] // ATOMS
    cluster_grid = positions.reshape(positions.shape[0], 3, rows_total, cols_total, ATOMS)
    padded = jnp.pad(cluster_grid, ((0, 0), (0, 0), (1, 1), (1, 1), (0, 0)))
    flag_all = bonds.astype(jnp.float32)
    ones_flag = jnp.ones((cols_total,), jnp.float32)

    def replica_force(padded_rep):
        def row_force(row_index):
            window = lax.dynamic_slice_in_dim(padded_rep, row_index, 3, 1)
            own_atoms = window[:, 1, 1:cols_total + 1]
            flag_row = lax.dynamic_index_in_dim(flag_all, row_index, 0, keepdims=False)
            summed = tile_forces(own_atoms, own_atoms, ones_flag, 0, 0)[0]
            for offset_index, (shift_x, shift_y) in enumerate(offsets_list):
                neighbour = window[:, 1 + shift_x, 1 + shift_y:1 + shift_y + cols_total]
                summed = summed + tile_forces(own_atoms, neighbour, flag_row[:, offset_index], shift_x, shift_y)[0]
            return summed

        return lax.map(row_force, jnp.arange(rows_total, dtype=jnp.int32))

    forces = lax.map(replica_force, padded)
    averaged = jnp.sum(forces, axis=0) / N_REP
    mean_force = jnp.transpose(averaged, (1, 0, 2, 3)).reshape(3, rows_total, cols_total * ATOMS)
    new_velocity = friction * velocities + time_step * mean_force[None] + noise_coef * noise
    new_position = positions + time_step * new_velocity
    return mean_force, new_velocity, new_position
```

```python
import jax
import jax.numpy as jnp
from jax import lax
from jax.experimental import pallas as pl
from jax.experimental.pallas import tpu as pltpu
from jax.sharding import PartitionSpec as P

ATOMS = 64


spacing = 4.0
friction = 0.6
noise_coef = 0.8
time_step = 0.2
offsets_list = ((0, 1), (1, -1), (1, 0), (1, 1), (0, -1), (-1, 1), (-1, 0), (-1, -1))
LANES = 128


def passed_along(value, axis, steps):
    count = lax.axis_size(axis)
    leading, last = (max(0, -steps), min(count, count - steps))
    return lax.ppermute(value, axis, [(source, source + steps) for source in range(leading, last)])


def ring_shift(value, axis, steps):
    count = lax.axis_size(axis)
    return lax.ppermute(value, axis, [(source, (source + steps) % count) for source in range(count)])


def force_kernel(rows, pairs, chunks, own_ref, halo_ref, flag_ref, out_ref, cbuf):
    n_blocks = 2 * pairs + 1
    left = lax.broadcasted_iota(jnp.int32, (ATOMS, LANES), 1) < ATOMS

    def build(h, slot):
        for c in range(3):
            prev = None
            for t in range(chunks):
                if 2 * t - 1 >= n_blocks:
                    break
                r = halo_ref[h, c : c + 1, t * LANES : (t + 1) * LANES]
                tt = jnp.transpose(jnp.broadcast_to(r, (LANES, LANES)))
                if prev is not None and 2 * t - 1 < n_blocks:
                    cbuf[slot, c, 2 * t - 1] = jnp.where(left, prev[ATOMS:], tt[:ATOMS])
                if 2 * t < n_blocks:
                    cbuf[slot, c, 2 * t] = jnp.where(left, tt[:ATOMS], tt[ATOMS:])
                prev = tt

    build(0, 0)
    build(1, 1)

    offsets = ((0, 0),) + offsets_list

    def row_body(i, carry):
        build(i + 2, lax.rem(i + 2, 3))

        def pair_body(k, carry2):
            base = pl.multiple_of(k * LANES, LANES)
            own = own_ref[i, :, pl.ds(base, LANES)]
            flags = flag_ref[i, :, pl.ds(base, LANES)]
            acc = [jnp.zeros((8, LANES), jnp.float32) for _ in range(3)]
            for oi, (dx, dy) in enumerate(offsets):
                slot = lax.rem(i + 1 + dx, 3)
                n = 2 * k + 1 + dy
                if oi == 0:
                    f2 = jnp.full((8, LANES), 2.0, jnp.float32)
                    fh = jnp.full((8, LANES), 0.5, jnp.float32)
                else:
                    f = jnp.broadcast_to(flags[oi - 1 : oi], (8, LANES))
                    f2 = 2.0 * f
                    fh = 0.5 * f
                xs = jnp.broadcast_to(own[0:1] - dx * spacing, (8, LANES))
                ys = jnp.broadcast_to(own[1:2] - dy * spacing, (8, LANES))
                zs = jnp.broadcast_to(own[2:3], (8, LANES))
                for r in range(ATOMS // 8):
                    cx = cbuf[slot, 0, n, r * 8 : (r + 1) * 8, :]
                    cy = cbuf[slot, 1, n, r * 8 : (r + 1) * 8, :]
                    cz = cbuf[slot, 2, n, r * 8 : (r + 1) * 8, :]
                    ddx = xs - cx
                    ddy = ys - cy
                    ddz = zs - cz
                    s = ddx * ddx + ddy * ddy + ddz * ddz
                    a = jnp.exp(-0.5 * s)
                    a2 = a * a
                    w = f2 * (a2 * a2) - fh * a
                    acc[0] = acc[0] + w * ddx
                    acc[1] = acc[1] + w * ddy
                    acc[2] = acc[2] + w * ddz
            for c in range(3):
                out_ref[i, c : c + 1, pl.ds(base, LANES)] = jnp.sum(acc[c], axis=0, keepdims=True)
            return carry2

        lax.fori_loop(0, pairs, pair_body, 0)
        return carry

    lax.fori_loop(0, rows, row_body, 0)


def cluster_forces(own, halo, flags):
    rows, _, width = own.shape
    pairs = width // LANES
    chunks = halo.shape[2] // LANES
    n_blocks = 2 * pairs + 1
    kernel = lambda *refs: force_kernel(rows, pairs, chunks, *refs)
    pair_count = rows * pairs * 9 * ATOMS * LANES
    return pl.pallas_call(
        kernel,
        out_shape=jax.ShapeDtypeStruct(own.shape, jnp.float32),
        in_specs=[pl.BlockSpec(memory_space=pltpu.VMEM)] * 3,
        out_specs=pl.BlockSpec(memory_space=pltpu.VMEM),
        scratch_shapes=[pltpu.VMEM((3, 3, n_blocks, ATOMS, LANES), jnp.float32)],
        compiler_params=pltpu.CompilerParams(vmem_limit_bytes=48 * 1024 * 1024),
        cost_estimate=pl.CostEstimate(
            flops=20 * pair_count,
            transcendentals=pair_count,
            bytes_accessed=4 * (own.size * 2 + halo.size + flags.size),
        ),
    )(own, halo, flags)


def per_device(positions, velocities, noise, bonds):
    rows_local = positions.shape[2]
    cols_local = positions.shape[3] // ATOMS
    width = cols_local * ATOMS
    coords = positions[0]
    lower_col = passed_along(coords[:, :, width - ATOMS :], "gy", 1)
    upper_col = passed_along(coords[:, :, :ATOMS], "gy", -1)
    widened = jnp.concatenate([lower_col, coords, upper_col], axis=2)
    prev_row = passed_along(widened[:, rows_local - 1 :], "gx", 1)
    next_row = passed_along(widened[:, :1], "gx", -1)
    halo = jnp.concatenate([prev_row, widened, next_row], axis=1)
    chunks = -(-(width + 2 * ATOMS) // LANES)
    halo = jnp.pad(halo, ((0, 0), (0, 0), (0, chunks * LANES - width - 2 * ATOMS)))
    halo = jnp.transpose(halo, (1, 0, 2))
    own = jnp.transpose(coords, (1, 0, 2))
    flags = jnp.repeat(jnp.transpose(bonds.astype(jnp.float32), (0, 2, 1)), ATOMS, axis=2)
    force = jnp.transpose(cluster_forces(own, halo, flags), (1, 0, 2))
    across = ring_shift(force, "rep", 2)
    near = ring_shift(force, "rep", 1)
    far = ring_shift(force, "rep", 3)
    summed_force = (force + across) + (near + far)
    mean_force = summed_force / lax.axis_size("rep")
    new_velocity = friction * velocities + time_step * mean_force[None] + noise_coef * noise
    new_position = positions + time_step * new_velocity
    return (mean_force, new_velocity, new_position)


def solution(mesh):
    in_specs = (
        P("rep", None, "gx", "gy"),
        P("rep", None, "gx", "gy"),
        P("rep", None, "gx", "gy"),
        P("gx", "gy", None),
    )
    out_specs = (P(None, "gx", "gy"), P("rep", None, "gx", "gy"), P("rep", None, "gx", "gy"))
    return jax.shard_map(
        per_device, mesh=mesh, in_specs=in_specs, out_specs=out_specs, check_vma=False
    )
```

```python
import jax
import jax.numpy as jnp
from jax import lax
from jax.experimental import pallas as pl
from jax.experimental.pallas import tpu as pltpu
from jax.sharding import PartitionSpec as P

ATOMS = 64


spacing = 4.0
friction = 0.6
noise_coef = 0.8
time_step = 0.2
offsets_list = ((0, 1), (1, -1), (1, 0), (1, 1), (0, -1), (-1, 1), (-1, 0), (-1, -1))
LANES = 128


def passed_along(value, axis, steps):
    count = lax.axis_size(axis)
    leading, last = (max(0, -steps), min(count, count - steps))
    return lax.ppermute(value, axis, [(source, source + steps) for source in range(leading, last)])


def ring_shift(value, axis, steps):
    count = lax.axis_size(axis)
    return lax.ppermute(value, axis, [(source, (source + steps) % count) for source in range(count)])


def force_kernel(rows, pairs, chunks, fresh, stride, own_ref, halo_ref, flag_ref, out_ref, cbuf):
    n_blocks = 2 * chunks - 1
    left = lax.broadcasted_iota(jnp.int32, (ATOMS, LANES), 1) < ATOMS

    def build(h, slot):
        for c in range(3):
            prev = None
            for t in range(chunks):
                r = halo_ref[h, c : c + 1, t * LANES : (t + 1) * LANES]
                tt = jnp.transpose(jnp.broadcast_to(r, (LANES, LANES)))
                if prev is not None:
                    cbuf[slot, c, 2 * t - 1] = jnp.where(left, prev[ATOMS:], tt[:ATOMS])
                cbuf[slot, c, 2 * t] = jnp.where(left, tt[:ATOMS], tt[ATOMS:])
                prev = tt

    if not fresh:
        build(0, 0)
        build(1, 1)

    offsets = ((0, 0),) + offsets_list

    def row_body(i, carry):
        if fresh:
            for j in range(3):
                build(3 * i + j, j)
        else:
            build(i + 2, lax.rem(i + 2, 3))

        def pair_body(k, carry2):
            base = pl.multiple_of(k * LANES, LANES)
            own = own_ref[i, :, pl.ds(base, LANES)]
            flags = flag_ref[i, :, pl.ds(base, LANES)]
            acc = [jnp.zeros((8, LANES), jnp.float32) for _ in range(3)]
            for oi, (dx, dy) in enumerate(offsets):
                slot = dx + 1 if fresh else lax.rem(i + 1 + dx, 3)
                n = stride * k + 1 + dy
                if oi == 0:
                    f2 = jnp.full((8, LANES), 2.0, jnp.float32)
                    fh = jnp.full((8, LANES), 0.5, jnp.float32)
                else:
                    f = jnp.broadcast_to(flags[oi - 1 : oi], (8, LANES))
                    f2 = 2.0 * f
                    fh = 0.5 * f
                xs = jnp.broadcast_to(own[0:1] - dx * spacing, (8, LANES))
                ys = jnp.broadcast_to(own[1:2] - dy * spacing, (8, LANES))
                zs = jnp.broadcast_to(own[2:3], (8, LANES))
                for r in range(ATOMS // 8):
                    cx = cbuf[slot, 0, n, r * 8 : (r + 1) * 8, :]
                    cy = cbuf[slot, 1, n, r * 8 : (r + 1) * 8, :]
                    cz = cbuf[slot, 2, n, r * 8 : (r + 1) * 8, :]
                    ddx = xs - cx
                    ddy = ys - cy
                    ddz = zs - cz
                    s = ddx * ddx + ddy * ddy + ddz * ddz
                    a = jnp.exp(-0.5 * s)
                    a2 = a * a
                    w = f2 * (a2 * a2) - fh * a
                    acc[0] = acc[0] + w * ddx
                    acc[1] = acc[1] + w * ddy
                    acc[2] = acc[2] + w * ddz
            for c in range(3):
                out_ref[i, c : c + 1, pl.ds(base, LANES)] = jnp.sum(acc[c], axis=0, keepdims=True)
            return carry2

        lax.fori_loop(0, pairs, pair_body, 0)
        return carry

    lax.fori_loop(0, rows, row_body, 0)


def cluster_forces(own, halo, flags, fresh=False, stride=2):
    rows, _, width = own.shape
    pairs = width // LANES
    chunks = halo.shape[2] // LANES
    n_blocks = 2 * chunks - 1
    kernel = lambda *refs: force_kernel(rows, pairs, chunks, fresh, stride, *refs)
    pair_count = rows * pairs * 9 * ATOMS * LANES
    return pl.pallas_call(
        kernel,
        out_shape=jax.ShapeDtypeStruct(own.shape, jnp.float32),
        in_specs=[pl.BlockSpec(memory_space=pltpu.VMEM)] * 3,
        out_specs=pl.BlockSpec(memory_space=pltpu.VMEM),
        scratch_shapes=[pltpu.VMEM((3, 3, n_blocks, ATOMS, LANES), jnp.float32)],
        compiler_params=pltpu.CompilerParams(vmem_limit_bytes=48 * 1024 * 1024),
        cost_estimate=pl.CostEstimate(
            flops=20 * pair_count,
            transcendentals=pair_count,
            bytes_accessed=4 * (own.size * 2 + halo.size + flags.size),
        ),
    )(own, halo, flags)


def diagonal(value, steps_x, steps_y):
    count_x, count_y = lax.axis_size("gx"), lax.axis_size("gy")
    pairs = []
    for source_x in range(count_x):
        for source_y in range(count_y):
            target_x, target_y = source_x + steps_x, source_y + steps_y
            if 0 <= target_x < count_x and 0 <= target_y < count_y:
                pairs.append((source_x * count_y + source_y, target_x * count_y + target_y))
    return lax.ppermute(value, ("gx", "gy"), pairs)


def replica_sum(force):
    across = ring_shift(force, "rep", 2)
    near = ring_shift(force, "rep", 1)
    far = ring_shift(force, "rep", 3)
    return (force + across) + (near + far)


def per_device(positions, velocities, noise, bonds):
    rows = positions.shape[2]
    width = positions.shape[3]
    coords = positions[0]
    own = jnp.transpose(coords, (1, 0, 2))
    flags = jnp.repeat(jnp.transpose(bonds.astype(jnp.float32), (0, 2, 1)), ATOMS, axis=2)
    inner = cluster_forces(
        own[1 : rows - 1, :, LANES : width - LANES],
        own[:, :, ATOMS : width - ATOMS],
        flags[1 : rows - 1, :, LANES : width - LANES],
    )
    lower_col = passed_along(coords[:, :, width - ATOMS :], "gy", 1)
    upper_col = passed_along(coords[:, :, :ATOMS], "gy", -1)
    prev_body = passed_along(coords[:, rows - 1 :], "gx", 1)
    next_body = passed_along(coords[:, :1], "gx", -1)
    prev_low = diagonal(coords[:, rows - 1 :, width - ATOMS :], 1, 1)
    prev_high = diagonal(coords[:, rows - 1 :, :ATOMS], 1, -1)
    next_low = diagonal(coords[:, :1, width - ATOMS :], -1, 1)
    next_high = diagonal(coords[:, :1, :ATOMS], -1, -1)
    pieces = (lower_col, upper_col, prev_body, next_body, prev_low, prev_high, next_low, next_high)
    inner, pieces = lax.optimization_barrier((inner, pieces))
    inner_sum = replica_sum(inner)
    lower_col, upper_col, prev_body, next_body, prev_low, prev_high, next_low, next_high = pieces
    widened = jnp.concatenate([lower_col, coords, upper_col], axis=2)
    prev_row = jnp.concatenate([prev_low, prev_body, prev_high], axis=2)
    next_row = jnp.concatenate([next_low, next_body, next_high], axis=2)
    halo = jnp.transpose(jnp.concatenate([prev_row, widened, next_row], axis=1), (1, 0, 2))
    edge_rows = cluster_forces(
        jnp.concatenate([own[:1], own[rows - 1 :]], axis=0),
        jnp.concatenate([halo[:3], halo[rows - 1 :]], axis=0),
        jnp.concatenate([flags[:1], flags[rows - 1 :]], axis=0),
        fresh=True,
    )
    edge_cols = cluster_forces(
        jnp.concatenate([own[1 : rows - 1, :, :LANES], own[1 : rows - 1, :, width - LANES :]], axis=2),
        jnp.concatenate([halo[1 : rows + 1, :, : 2 * LANES], halo[1 : rows + 1, :, width - 2 * LANES + 2 * ATOMS :]], axis=2),
        jnp.concatenate([flags[1 : rows - 1, :, :LANES], flags[1 : rows - 1, :, width - LANES :]], axis=2),
        stride=4,
    )
    edge_sum = replica_sum(
        jnp.concatenate([edge_rows.reshape(-1, LANES), edge_cols.reshape(-1, LANES)], axis=0)
    )
    n_rows_part = edge_rows.size // LANES
    rows_sum = edge_sum[:n_rows_part].reshape(edge_rows.shape)
    cols_sum = edge_sum[n_rows_part:].reshape(edge_cols.shape)
    middle = jnp.concatenate([cols_sum[:, :, :LANES], inner_sum, cols_sum[:, :, LANES:]], axis=2)
    summed_force = jnp.concatenate([rows_sum[:1], middle, rows_sum[1:]], axis=0)
    summed_force = jnp.transpose(summed_force, (1, 0, 2))
    mean_force = summed_force / lax.axis_size("rep")
    new_velocity = friction * velocities + time_step * mean_force[None] + noise_coef * noise
    new_position = positions + time_step * new_velocity
    return (mean_force, new_velocity, new_position)


def solution(mesh):
    in_specs = (
        P("rep", None, "gx", "gy"),
        P("rep", None, "gx", "gy"),
        P("rep", None, "gx", "gy"),
        P("gx", "gy", None),
    )
    out_specs = (P(None, "gx", "gy"), P("rep", None, "gx", "gy"), P("rep", None, "gx", "gy"))
    return jax.shard_map(
        per_device, mesh=mesh, in_specs=in_specs, out_specs=out_specs, check_vma=False
    )
```

```python
import jax
import jax.numpy as jnp
from jax import lax
from jax.experimental import pallas as pl
from jax.experimental.pallas import tpu as pltpu
from jax.sharding import PartitionSpec as P

ATOMS = 64


spacing = 4.0
friction = 0.6
noise_coef = 0.8
time_step = 0.2
offsets_list = ((0, 1), (1, -1), (1, 0), (1, 1), (0, -1), (-1, 1), (-1, 0), (-1, -1))
LANES = 128


def passed_along(value, axis, steps):
    count = lax.axis_size(axis)
    leading, last = (max(0, -steps), min(count, count - steps))
    return lax.ppermute(value, axis, [(source, source + steps) for source in range(leading, last)])


def ring_shift(value, axis, steps):
    count = lax.axis_size(axis)
    return lax.ppermute(value, axis, [(source, (source + steps) % count) for source in range(count)])


def force_kernel(rows, pairs, chunks, own_ref, halo_ref, flag_ref, out_ref, cbuf):
    n_blocks = 2 * pairs + 1
    left = lax.broadcasted_iota(jnp.int32, (ATOMS, LANES), 1) < ATOMS

    def build(h, slot):
        for c in range(3):
            prev = None
            for t in range(chunks):
                if 2 * t - 1 >= n_blocks:
                    break
                r = halo_ref[h, c : c + 1, t * LANES : (t + 1) * LANES]
                tt = jnp.transpose(jnp.broadcast_to(r, (LANES, LANES)))
                if prev is not None and 2 * t - 1 < n_blocks:
                    cbuf[slot, c, 2 * t - 1] = jnp.where(left, prev[ATOMS:], tt[:ATOMS])
                if 2 * t < n_blocks:
                    cbuf[slot, c, 2 * t] = jnp.where(left, tt[:ATOMS], tt[ATOMS:])
                prev = tt

    build(0, 0)
    build(1, 1)

    offsets = ((0, 0),) + offsets_list

    def row_body(i, carry):
        build(i + 2, lax.rem(i + 2, 3))

        def pair_body(k, carry2):
            base = pl.multiple_of(k * LANES, LANES)
            own = own_ref[i, :, pl.ds(base, LANES)]
            flags = flag_ref[i, :, pl.ds(base, LANES)]
            acc = [jnp.zeros((8, LANES), jnp.float32) for _ in range(3)]
            for oi, (dx, dy) in enumerate(offsets):
                slot = lax.rem(i + 1 + dx, 3)
                n = 2 * k + 1 + dy
                if oi == 0:
                    f2 = jnp.full((8, LANES), 2.0, jnp.float32)
                    fh = jnp.full((8, LANES), 0.5, jnp.float32)
                else:
                    f = jnp.broadcast_to(flags[oi - 1 : oi], (8, LANES))
                    f2 = 2.0 * f
                    fh = 0.5 * f
                xs = jnp.broadcast_to(own[0:1] - dx * spacing, (8, LANES))
                ys = jnp.broadcast_to(own[1:2] - dy * spacing, (8, LANES))
                zs = jnp.broadcast_to(own[2:3], (8, LANES))
                for r in range(ATOMS // 8):
                    cx = cbuf[slot, 0, n, r * 8 : (r + 1) * 8, :]
                    cy = cbuf[slot, 1, n, r * 8 : (r + 1) * 8, :]
                    cz = cbuf[slot, 2, n, r * 8 : (r + 1) * 8, :]
                    ddx = xs - cx
                    ddy = ys - cy
                    ddz = zs - cz
                    s = ddx * ddx + ddy * ddy + ddz * ddz
                    a = jnp.exp(-0.5 * s)
                    a2 = a * a
                    w = f2 * (a2 * a2) - fh * a
                    acc[0] = acc[0] + w * ddx
                    acc[1] = acc[1] + w * ddy
                    acc[2] = acc[2] + w * ddz
            for c in range(3):
                out_ref[i, c : c + 1, pl.ds(base, LANES)] = jnp.sum(acc[c], axis=0, keepdims=True)
            return carry2

        lax.fori_loop(0, pairs, pair_body, 0)
        return carry

    lax.fori_loop(0, rows, row_body, 0)


def cluster_forces(own, halo, flags):
    rows, _, width = own.shape
    pairs = width // LANES
    chunks = halo.shape[2] // LANES
    n_blocks = 2 * pairs + 1
    kernel = lambda *refs: force_kernel(rows, pairs, chunks, *refs)
    pair_count = rows * pairs * 9 * ATOMS * LANES
    return pl.pallas_call(
        kernel,
        out_shape=jax.ShapeDtypeStruct(own.shape, jnp.float32),
        in_specs=[pl.BlockSpec(memory_space=pltpu.VMEM)] * 3,
        out_specs=pl.BlockSpec(memory_space=pltpu.VMEM),
        scratch_shapes=[pltpu.VMEM((3, 3, n_blocks, ATOMS, LANES), jnp.float32)],
        compiler_params=pltpu.CompilerParams(vmem_limit_bytes=48 * 1024 * 1024),
        cost_estimate=pl.CostEstimate(
            flops=20 * pair_count,
            transcendentals=pair_count,
            bytes_accessed=4 * (own.size * 2 + halo.size + flags.size),
        ),
    )(own, halo, flags)


def per_device(positions, velocities, noise, bonds):
    rows_local = positions.shape[2]
    cols_local = positions.shape[3] // ATOMS
    width = cols_local * ATOMS
    coords = positions[0]
    lower_col = passed_along(coords[:, :, width - ATOMS :], "gy", 1)
    upper_col = passed_along(coords[:, :, :ATOMS], "gy", -1)
    widened = jnp.concatenate([lower_col, coords, upper_col], axis=2)
    prev_row = passed_along(widened[:, rows_local - 1 :], "gx", 1)
    next_row = passed_along(widened[:, :1], "gx", -1)
    halo = jnp.concatenate([prev_row, widened, next_row], axis=1)
    chunks = -(-(width + 2 * ATOMS) // LANES)
    halo = jnp.pad(halo, ((0, 0), (0, 0), (0, chunks * LANES - width - 2 * ATOMS)))
    halo = jnp.transpose(halo, (1, 0, 2))
    own = jnp.transpose(coords, (1, 0, 2))
    flags = jnp.repeat(jnp.transpose(bonds.astype(jnp.float32), (0, 2, 1)), ATOMS, axis=2)
    force = jnp.transpose(cluster_forces(own, halo, flags), (1, 0, 2))
    paired = force + ring_shift(force, "rep", 2)
    summed_force = paired + ring_shift(paired, "rep", 1)
    mean_force = summed_force / lax.axis_size("rep")
    new_velocity = friction * velocities + time_step * mean_force[None] + noise_coef * noise
    new_position = positions + time_step * new_velocity
    return (mean_force, new_velocity, new_position)


def solution(mesh):
    in_specs = (
        P("rep", None, "gx", "gy"),
        P("rep", None, "gx", "gy"),
        P("rep", None, "gx", "gy"),
        P("gx", "gy", None),
    )
    out_specs = (P(None, "gx", "gy"), P("rep", None, "gx", "gy"), P("rep", None, "gx", "gy"))
    return jax.shard_map(
        per_device, mesh=mesh, in_specs=in_specs, out_specs=out_specs, check_vma=False
    )
```

```python
import math

import jax
import jax.numpy as jnp
from jax import lax
from jax.experimental import pallas as pl
from jax.experimental.pallas import tpu as pltpu
from jax.sharding import PartitionSpec as P

ATOMS = 64


spacing = 4.0
friction = 0.6
noise_coef = 0.8
time_step = 0.2
offsets_list = ((0, 1), (1, -1), (1, 0), (1, 1), (0, -1), (-1, 1), (-1, 0), (-1, -1))
LANES = 128
SCALE = math.sqrt(0.5 * math.log2(math.e))


def passed_along(value, axis, steps):
    count = lax.axis_size(axis)
    leading, last = (max(0, -steps), min(count, count - steps))
    return lax.ppermute(value, axis, [(source, source + steps) for source in range(leading, last)])


def ring_shift(value, axis, steps):
    count = lax.axis_size(axis)
    return lax.ppermute(value, axis, [(source, (source + steps) % count) for source in range(count)])


def force_kernel(rows, pairs, chunks, own_ref, halo_ref, flag_ref, out_ref, cbuf):
    n_blocks = 2 * pairs + 1
    left = lax.broadcasted_iota(jnp.int32, (ATOMS, LANES), 1) < ATOMS

    def build(h, slot):
        for c in range(3):
            prev = None
            for t in range(chunks):
                if 2 * t - 1 >= n_blocks:
                    break
                r = halo_ref[h, c : c + 1, t * LANES : (t + 1) * LANES]
                tt = jnp.transpose(jnp.broadcast_to(r, (LANES, LANES)))
                if prev is not None and 2 * t - 1 < n_blocks:
                    cbuf[slot, c, 2 * t - 1] = jnp.where(left, prev[ATOMS:], tt[:ATOMS])
                if 2 * t < n_blocks:
                    cbuf[slot, c, 2 * t] = jnp.where(left, tt[:ATOMS], tt[ATOMS:])
                prev = tt

    build(0, 0)
    build(1, 1)

    offsets = ((0, 0),) + offsets_list

    def row_body(i, carry):
        build(i + 2, lax.rem(i + 2, 3))

        def pair_body(k, carry2):
            base = pl.multiple_of(k * LANES, LANES)
            own = own_ref[i, :, pl.ds(base, LANES)]
            flags = flag_ref[i, :, pl.ds(base, LANES)]
            acc = [jnp.zeros((8, LANES), jnp.float32) for _ in range(3)]
            for oi, (dx, dy) in enumerate(offsets):
                slot = lax.rem(i + 1 + dx, 3)
                n = 2 * k + 1 + dy
                if oi == 0:
                    f2 = jnp.full((8, LANES), 2.0, jnp.float32)
                    fh = jnp.full((8, LANES), 0.5, jnp.float32)
                else:
                    f = jnp.broadcast_to(flags[oi - 1 : oi], (8, LANES))
                    f2 = 2.0 * f
                    fh = 0.5 * f
                xs = jnp.broadcast_to(own[0:1] - dx * spacing * SCALE, (8, LANES))
                ys = jnp.broadcast_to(own[1:2] - dy * spacing * SCALE, (8, LANES))
                zs = jnp.broadcast_to(own[2:3], (8, LANES))
                for r in range(ATOMS // 8):
                    cx = cbuf[slot, 0, n, r * 8 : (r + 1) * 8, :]
                    cy = cbuf[slot, 1, n, r * 8 : (r + 1) * 8, :]
                    cz = cbuf[slot, 2, n, r * 8 : (r + 1) * 8, :]
                    ddx = xs - cx
                    ddy = ys - cy
                    ddz = zs - cz
                    t = -(ddx * ddx) - ddy * ddy - ddz * ddz
                    w = f2 * jnp.exp2(4.0 * t) - fh * jnp.exp2(t)
                    acc[0] = acc[0] + w * ddx
                    acc[1] = acc[1] + w * ddy
                    acc[2] = acc[2] + w * ddz
            for c in range(3):
                out_ref[i, c : c + 1, pl.ds(base, LANES)] = jnp.sum(acc[c], axis=0, keepdims=True) * (1.0 / SCALE)
            return carry2

        lax.fori_loop(0, pairs, pair_body, 0)
        return carry

    lax.fori_loop(0, rows, row_body, 0)


def cluster_forces(own, halo, flags):
    rows, _, width = own.shape
    pairs = width // LANES
    chunks = halo.shape[2] // LANES
    n_blocks = 2 * pairs + 1
    kernel = lambda *refs: force_kernel(rows, pairs, chunks, *refs)
    pair_count = rows * pairs * 9 * ATOMS * LANES
    return pl.pallas_call(
        kernel,
        out_shape=jax.ShapeDtypeStruct(own.shape, jnp.float32),
        in_specs=[pl.BlockSpec(memory_space=pltpu.VMEM)] * 3,
        out_specs=pl.BlockSpec(memory_space=pltpu.VMEM),
        scratch_shapes=[pltpu.VMEM((3, 3, n_blocks, ATOMS, LANES), jnp.float32)],
        compiler_params=pltpu.CompilerParams(vmem_limit_bytes=48 * 1024 * 1024),
        cost_estimate=pl.CostEstimate(
            flops=20 * pair_count,
            transcendentals=pair_count,
            bytes_accessed=4 * (own.size * 2 + halo.size + flags.size),
        ),
    )(own, halo, flags)


def per_device(positions, velocities, noise, bonds):
    rows_local = positions.shape[2]
    cols_local = positions.shape[3] // ATOMS
    width = cols_local * ATOMS
    coords = positions[0]
    lower_col = passed_along(coords[:, :, width - ATOMS :], "gy", 1)
    upper_col = passed_along(coords[:, :, :ATOMS], "gy", -1)
    widened = jnp.concatenate([lower_col, coords, upper_col], axis=2)
    prev_row = passed_along(widened[:, rows_local - 1 :], "gx", 1)
    next_row = passed_along(widened[:, :1], "gx", -1)
    halo = jnp.concatenate([prev_row, widened, next_row], axis=1)
    chunks = -(-(width + 2 * ATOMS) // LANES)
    halo = jnp.pad(halo, ((0, 0), (0, 0), (0, chunks * LANES - width - 2 * ATOMS)))
    halo = jnp.transpose(halo, (1, 0, 2)) * SCALE
    own = jnp.transpose(coords, (1, 0, 2)) * SCALE
    flags = jnp.repeat(jnp.transpose(bonds.astype(jnp.float32), (0, 2, 1)), ATOMS, axis=2)
    force = jnp.transpose(cluster_forces(own, halo, flags), (1, 0, 2))
    across = ring_shift(force, "rep", 2)
    near = ring_shift(force, "rep", 1)
    far = ring_shift(force, "rep", 3)
    summed_force = (force + across) + (near + far)
    mean_force = summed_force / lax.axis_size("rep")
    new_velocity = friction * velocities + time_step * mean_force[None] + noise_coef * noise
    new_position = positions + time_step * new_velocity
    return (mean_force, new_velocity, new_position)


def solution(mesh):
    in_specs = (
        P("rep", None, "gx", "gy"),
        P("rep", None, "gx", "gy"),
        P("rep", None, "gx", "gy"),
        P("gx", "gy", None),
    )
    out_specs = (P(None, "gx", "gy"), P("rep", None, "gx", "gy"), P("rep", None, "gx", "gy"))
    return jax.shard_map(
        per_device, mesh=mesh, in_specs=in_specs, out_specs=out_specs, check_vma=False
    )
```

```python
import math

import jax
import jax.numpy as jnp
from jax import lax
from jax.experimental import pallas as pl
from jax.experimental.pallas import tpu as pltpu
from jax.sharding import PartitionSpec as P

ATOMS = 64


spacing = 4.0
friction = 0.6
noise_coef = 0.8
time_step = 0.2
offsets_list = ((0, 1), (1, -1), (1, 0), (1, 1), (0, -1), (-1, 1), (-1, 0), (-1, -1))
LANES = 128
SCALE = math.sqrt(0.5 * math.log2(math.e))


def passed_along(value, axis, steps):
    count = lax.axis_size(axis)
    leading, last = (max(0, -steps), min(count, count - steps))
    return lax.ppermute(value, axis, [(source, source + steps) for source in range(leading, last)])


def ring_shift(value, axis, steps):
    count = lax.axis_size(axis)
    return lax.ppermute(value, axis, [(source, (source + steps) % count) for source in range(count)])


def force_kernel(rows, pairs, chunks, own_ref, halo_ref, flag_ref, out_ref, cbuf):
    n_blocks = 2 * pairs + 1
    left = lax.broadcasted_iota(jnp.int32, (ATOMS, LANES), 1) < ATOMS

    def build(h, slot):
        for c in range(3):
            prev = None
            for t in range(chunks):
                if 2 * t - 1 >= n_blocks:
                    break
                r = halo_ref[h, c : c + 1, t * LANES : (t + 1) * LANES]
                tt = jnp.transpose(jnp.broadcast_to(r, (LANES, LANES)))
                if prev is not None and 2 * t - 1 < n_blocks:
                    cbuf[slot, c, 2 * t - 1] = jnp.where(left, prev[ATOMS:], tt[:ATOMS])
                if 2 * t < n_blocks:
                    cbuf[slot, c, 2 * t] = jnp.where(left, tt[:ATOMS], tt[ATOMS:])
                prev = tt

    build(0, 0)
    build(1, 1)

    offsets = ((0, 0),) + offsets_list

    def row_body(i, carry):
        build(i + 2, lax.rem(i + 2, 3))

        def pair_body(k, carry2):
            base = pl.multiple_of(k * LANES, LANES)
            own = own_ref[i, :, pl.ds(base, LANES)]
            flags = flag_ref[i, :, pl.ds(base, LANES)]
            acc = [jnp.zeros((8, LANES), jnp.float32) for _ in range(3)]
            for oi, (dx, dy) in enumerate(offsets):
                slot = lax.rem(i + 1 + dx, 3)
                n = 2 * k + 1 + dy
                if oi == 0:
                    f2 = jnp.full((8, LANES), 2.0, jnp.float32)
                    fh = jnp.full((8, LANES), 0.5, jnp.float32)
                else:
                    f = jnp.broadcast_to(flags[oi - 1 : oi], (8, LANES))
                    f2 = 2.0 * f
                    fh = 0.5 * f
                xs = jnp.broadcast_to(own[0:1] - dx * spacing * SCALE, (8, LANES))
                ys = jnp.broadcast_to(own[1:2] - dy * spacing * SCALE, (8, LANES))
                zs = jnp.broadcast_to(own[2:3], (8, LANES))
                for r in range(ATOMS // 8):
                    cx = cbuf[slot, 0, n, r * 8 : (r + 1) * 8, :]
                    cy = cbuf[slot, 1, n, r * 8 : (r + 1) * 8, :]
                    cz = cbuf[slot, 2, n, r * 8 : (r + 1) * 8, :]
                    ddx = xs - cx
                    ddy = ys - cy
                    ddz = zs - cz
                    t = -(ddx * ddx) - ddy * ddy - ddz * ddz
                    w = f2 * jnp.exp2(4.0 * t) - fh * jnp.exp2(t)
                    acc[0] = acc[0] + w * ddx
                    acc[1] = acc[1] + w * ddy
                    acc[2] = acc[2] + w * ddz
            for c in range(3):
                out_ref[i, c : c + 1, pl.ds(base, LANES)] = jnp.sum(acc[c], axis=0, keepdims=True) * (1.0 / SCALE)
            return carry2

        lax.fori_loop(0, pairs, pair_body, 0)
        return carry

    lax.fori_loop(0, rows, row_body, 0)


def cluster_forces(own, halo, flags):
    rows, _, width = own.shape
    pairs = width // LANES
    chunks = halo.shape[2] // LANES
    n_blocks = 2 * pairs + 1
    kernel = lambda *refs: force_kernel(rows, pairs, chunks, *refs)
    pair_count = rows * pairs * 9 * ATOMS * LANES
    return pl.pallas_call(
        kernel,
        out_shape=jax.ShapeDtypeStruct(own.shape, jnp.float32),
        in_specs=[pl.BlockSpec(memory_space=pltpu.VMEM)] * 3,
        out_specs=pl.BlockSpec(memory_space=pltpu.VMEM),
        scratch_shapes=[pltpu.VMEM((3, 3, n_blocks, ATOMS, LANES), jnp.float32)],
        compiler_params=pltpu.CompilerParams(vmem_limit_bytes=48 * 1024 * 1024),
        cost_estimate=pl.CostEstimate(
            flops=20 * pair_count,
            transcendentals=pair_count,
            bytes_accessed=4 * (own.size * 2 + halo.size + flags.size),
        ),
    )(own, halo, flags)


def per_device(positions, velocities, noise, bonds):
    rows_local = positions.shape[2]
    cols_local = positions.shape[3] // ATOMS
    width = cols_local * ATOMS
    coords = positions[0]
    lower_col = passed_along(coords[:, :, width - ATOMS :], "gy", 1)
    upper_col = passed_along(coords[:, :, :ATOMS], "gy", -1)
    widened = jnp.concatenate([lower_col, coords, upper_col], axis=2)
    prev_row = passed_along(widened[:, rows_local - 1 :], "gx", 1)
    next_row = passed_along(widened[:, :1], "gx", -1)
    halo = jnp.concatenate([prev_row, widened, next_row], axis=1)
    chunks = -(-(width + 2 * ATOMS) // LANES)
    halo = jnp.pad(halo, ((0, 0), (0, 0), (0, chunks * LANES - width - 2 * ATOMS)))
    halo = jnp.transpose(halo, (1, 0, 2)) * SCALE
    own = jnp.transpose(coords, (1, 0, 2)) * SCALE
    flags = jnp.repeat(jnp.transpose(bonds.astype(jnp.float32), (0, 2, 1)), ATOMS, axis=2)
    force = jnp.transpose(cluster_forces(own, halo, flags), (1, 0, 2))
    gathered = lax.all_gather(force, "rep")
    summed_force = (gathered[0] + gathered[2]) + (gathered[1] + gathered[3])
    mean_force = summed_force / lax.axis_size("rep")
    new_velocity = friction * velocities + time_step * mean_force[None] + noise_coef * noise
    new_position = positions + time_step * new_velocity
    return (mean_force, new_velocity, new_position)


def solution(mesh):
    in_specs = (
        P("rep", None, "gx", "gy"),
        P("rep", None, "gx", "gy"),
        P("rep", None, "gx", "gy"),
        P("gx", "gy", None),
    )
    out_specs = (P(None, "gx", "gy"), P("rep", None, "gx", "gy"), P("rep", None, "gx", "gy"))
    return jax.shard_map(
        per_device, mesh=mesh, in_specs=in_specs, out_specs=out_specs, check_vma=False
    )
```

```python
import math

import jax
import jax.numpy as jnp
from jax import lax
from jax.experimental import pallas as pl
from jax.experimental.pallas import tpu as pltpu
from jax.sharding import PartitionSpec as P

ATOMS = 64


spacing = 4.0
friction = 0.6
noise_coef = 0.8
time_step = 0.2
offsets_list = ((0, 1), (1, -1), (1, 0), (1, 1), (0, -1), (-1, 1), (-1, 0), (-1, -1))
LANES = 128
SCALE = math.sqrt(0.5 * math.log2(math.e))


def passed_along(value, axis, steps):
    count = lax.axis_size(axis)
    leading, last = (max(0, -steps), min(count, count - steps))
    return lax.ppermute(value, axis, [(source, source + steps) for source in range(leading, last)])


def ring_shift(value, axis, steps):
    count = lax.axis_size(axis)
    return lax.ppermute(value, axis, [(source, (source + steps) % count) for source in range(count)])


def force_kernel(rows, pairs, chunks, own_ref, halo_ref, flag_ref, out_ref, cbuf):
    n_blocks = 2 * pairs + 1
    left = lax.broadcasted_iota(jnp.int32, (ATOMS, LANES), 1) < ATOMS

    def build(h, slot):
        for c in range(3):
            prev = None
            for t in range(chunks):
                if 2 * t - 1 >= n_blocks:
                    break
                r = halo_ref[h, c : c + 1, t * LANES : (t + 1) * LANES]
                tt = jnp.transpose(jnp.broadcast_to(r, (LANES, LANES)))
                if prev is not None and 2 * t - 1 < n_blocks:
                    cbuf[slot, c, 2 * t - 1] = jnp.where(left, prev[ATOMS:], tt[:ATOMS])
                if 2 * t < n_blocks:
                    cbuf[slot, c, 2 * t] = jnp.where(left, tt[:ATOMS], tt[ATOMS:])
                prev = tt

    build(0, 0)
    build(1, 1)

    offsets = ((0, 0),) + offsets_list

    def row_body(i, carry):
        build(i + 2, lax.rem(i + 2, 3))

        def pair_body(k, carry2):
            base = pl.multiple_of(k * LANES, LANES)
            own = own_ref[i, :, pl.ds(base, LANES)]
            flags = flag_ref[i, :, pl.ds(base, LANES)]
            acc = [jnp.zeros((8, LANES), jnp.float32) for _ in range(3)]
            for oi, (dx, dy) in enumerate(offsets):
                slot = lax.rem(i + 1 + dx, 3)
                n = 2 * k + 1 + dy
                if oi == 0:
                    f2 = jnp.full((8, LANES), 2.0, jnp.float32)
                    fh = jnp.full((8, LANES), 0.5, jnp.float32)
                else:
                    f = jnp.broadcast_to(flags[oi - 1 : oi], (8, LANES))
                    f2 = 2.0 * f
                    fh = 0.5 * f
                xs = jnp.broadcast_to(own[0:1] - dx * spacing * SCALE, (8, LANES))
                ys = jnp.broadcast_to(own[1:2] - dy * spacing * SCALE, (8, LANES))
                zs = jnp.broadcast_to(own[2:3], (8, LANES))
                for r in range(ATOMS // 8):
                    cx = cbuf[slot, 0, n, r * 8 : (r + 1) * 8, :]
                    cy = cbuf[slot, 1, n, r * 8 : (r + 1) * 8, :]
                    cz = cbuf[slot, 2, n, r * 8 : (r + 1) * 8, :]
                    ddx = xs - cx
                    ddy = ys - cy
                    ddz = zs - cz
                    t = -(ddx * ddx) - ddy * ddy - ddz * ddz
                    w = f2 * jnp.exp2(4.0 * t) - fh * jnp.exp2(t)
                    acc[0] = acc[0] + w * ddx
                    acc[1] = acc[1] + w * ddy
                    acc[2] = acc[2] + w * ddz
            block = pl.multiple_of((i // 8) * 8, 8)
            mine = lax.broadcasted_iota(jnp.int32, (8, LANES), 0) == i % 8
            for c in range(3):
                row = jnp.sum(acc[c], axis=0, keepdims=True) * (1.0 / SCALE)
                held = out_ref[c, pl.ds(block, 8), pl.ds(base, LANES)]
                out_ref[c, pl.ds(block, 8), pl.ds(base, LANES)] = jnp.where(mine, row, held)
            return carry2

        lax.fori_loop(0, pairs, pair_body, 0)
        return carry

    lax.fori_loop(0, rows, row_body, 0)


def cluster_forces(own, halo, flags):
    rows, _, width = own.shape
    pairs = width // LANES
    chunks = halo.shape[2] // LANES
    n_blocks = 2 * pairs + 1
    kernel = lambda *refs: force_kernel(rows, pairs, chunks, *refs)
    pair_count = rows * pairs * 9 * ATOMS * LANES
    return pl.pallas_call(
        kernel,
        out_shape=jax.ShapeDtypeStruct((3, rows, width), jnp.float32),
        in_specs=[pl.BlockSpec(memory_space=pltpu.VMEM)] * 3,
        out_specs=pl.BlockSpec(memory_space=pltpu.VMEM),
        scratch_shapes=[pltpu.VMEM((3, 3, n_blocks, ATOMS, LANES), jnp.float32)],
        compiler_params=pltpu.CompilerParams(vmem_limit_bytes=48 * 1024 * 1024),
        cost_estimate=pl.CostEstimate(
            flops=20 * pair_count,
            transcendentals=pair_count,
            bytes_accessed=4 * (own.size * 2 + halo.size + flags.size),
        ),
    )(own, halo, flags)


def per_device(positions, velocities, noise, bonds):
    rows_local = positions.shape[2]
    cols_local = positions.shape[3] // ATOMS
    width = cols_local * ATOMS
    coords = positions[0]
    lower_col = passed_along(coords[:, :, width - ATOMS :], "gy", 1)
    upper_col = passed_along(coords[:, :, :ATOMS], "gy", -1)
    widened = jnp.concatenate([lower_col, coords, upper_col], axis=2)
    prev_row = passed_along(widened[:, rows_local - 1 :], "gx", 1)
    next_row = passed_along(widened[:, :1], "gx", -1)
    halo = jnp.concatenate([prev_row, widened, next_row], axis=1)
    chunks = -(-(width + 2 * ATOMS) // LANES)
    halo = jnp.pad(halo, ((0, 0), (0, 0), (0, chunks * LANES - width - 2 * ATOMS)))
    halo = jnp.transpose(halo, (1, 0, 2)) * SCALE
    own = jnp.transpose(coords, (1, 0, 2)) * SCALE
    flags = jnp.repeat(jnp.transpose(bonds.astype(jnp.float32), (0, 2, 1)), ATOMS, axis=2)
    force = cluster_forces(own, halo, flags)
    across = ring_shift(force, "rep", 2)
    near = ring_shift(force, "rep", 1)
    far = ring_shift(force, "rep", 3)
    summed_force = (force + across) + (near + far)
    mean_force = summed_force / lax.axis_size("rep")
    new_velocity = friction * velocities + time_step * mean_force[None] + noise_coef * noise
    new_position = positions + time_step * new_velocity
    return (mean_force, new_velocity, new_position)


def solution(mesh):
    in_specs = (
        P("rep", None, "gx", "gy"),
        P("rep", None, "gx", "gy"),
        P("rep", None, "gx", "gy"),
        P("gx", "gy", None),
    )
    out_specs = (P(None, "gx", "gy"), P("rep", None, "gx", "gy"), P("rep", None, "gx", "gy"))
    return jax.shard_map(
        per_device, mesh=mesh, in_specs=in_specs, out_specs=out_specs, check_vma=False
    )
```

```python
import math

import jax
import jax.numpy as jnp
from jax import lax
from jax.experimental import pallas as pl
from jax.experimental.pallas import tpu as pltpu
from jax.sharding import PartitionSpec as P

ATOMS = 64


spacing = 4.0
friction = 0.6
noise_coef = 0.8
time_step = 0.2
offsets_list = ((0, 1), (1, -1), (1, 0), (1, 1), (0, -1), (-1, 1), (-1, 0), (-1, -1))
LANES = 128
SCALE = math.sqrt(0.5 * math.log2(math.e))


def passed_along(value, axis, steps):
    count = lax.axis_size(axis)
    leading, last = (max(0, -steps), min(count, count - steps))
    return lax.ppermute(value, axis, [(source, source + steps) for source in range(leading, last)])


def ring_shift(value, axis, steps):
    count = lax.axis_size(axis)
    return lax.ppermute(value, axis, [(source, (source + steps) % count) for source in range(count)])


def force_kernel(rows, pairs, chunks, own_ref, halo_ref, flag_ref, out_ref, cbuf):
    n_blocks = 2 * pairs + 1
    left = lax.broadcasted_iota(jnp.int32, (ATOMS, LANES), 1) < ATOMS

    def build(h, slot):
        for c in range(3):
            prev = None
            for t in range(chunks):
                if 2 * t - 1 >= n_blocks:
                    break
                r = halo_ref[h, c : c + 1, t * LANES : (t + 1) * LANES]
                tt = jnp.transpose(jnp.broadcast_to(r, (LANES, LANES)))
                if prev is not None and 2 * t - 1 < n_blocks:
                    cbuf[slot, c, 2 * t - 1] = jnp.where(left, prev[ATOMS:], tt[:ATOMS])
                if 2 * t < n_blocks:
                    cbuf[slot, c, 2 * t] = jnp.where(left, tt[:ATOMS], tt[ATOMS:])
                prev = tt

    build(0, 0)
    build(1, 1)

    offsets = ((0, 0),) + offsets_list

    def row_body(i, carry):
        build(i + 2, lax.rem(i + 2, 3))

        def pair_body(k, carry2):
            base = pl.multiple_of(k * LANES, LANES)
            own = own_ref[i, :, pl.ds(base, LANES)]
            flags = flag_ref[i, :, pl.ds(base, LANES)]
            acc = [jnp.zeros((8, LANES), jnp.float32) for _ in range(3)]
            for oi, (dx, dy) in enumerate(offsets):
                slot = lax.rem(i + 1 + dx, 3)
                n = 2 * k + 1 + dy
                if oi == 0:
                    f2 = jnp.full((8, LANES), 2.0, jnp.float32)
                    fh = jnp.full((8, LANES), 0.5, jnp.float32)
                else:
                    f = jnp.broadcast_to(flags[oi - 1 : oi], (8, LANES))
                    f2 = 2.0 * f
                    fh = 0.5 * f
                xs = jnp.broadcast_to(own[0:1] - dx * spacing * SCALE, (8, LANES))
                ys = jnp.broadcast_to(own[1:2] - dy * spacing * SCALE, (8, LANES))
                zs = jnp.broadcast_to(own[2:3], (8, LANES))
                for r in range(ATOMS // 8):
                    cx = cbuf[slot, 0, n, r * 8 : (r + 1) * 8, :]
                    cy = cbuf[slot, 1, n, r * 8 : (r + 1) * 8, :]
                    cz = cbuf[slot, 2, n, r * 8 : (r + 1) * 8, :]
                    ddx = xs - cx
                    ddy = ys - cy
                    ddz = zs - cz
                    t = -(ddx * ddx) - ddy * ddy - ddz * ddz
                    w = f2 * jnp.exp2(4.0 * t) - fh * jnp.exp2(t)
                    acc[0] = acc[0] + w * ddx
                    acc[1] = acc[1] + w * ddy
                    acc[2] = acc[2] + w * ddz
            block = pl.multiple_of((i // 8) * 8, 8)
            mine = lax.broadcasted_iota(jnp.int32, (8, LANES), 0) == i % 8
            for c in range(3):
                row = jnp.sum(acc[c], axis=0, keepdims=True) * (1.0 / SCALE)
                held = out_ref[c, pl.ds(block, 8), pl.ds(base, LANES)]
                out_ref[c, pl.ds(block, 8), pl.ds(base, LANES)] = jnp.where(mine, row, held)
            return carry2

        lax.fori_loop(0, pairs, pair_body, 0)
        return carry

    lax.fori_loop(0, rows, row_body, 0)


def cluster_forces(own, halo, flags):
    rows, _, width = own.shape
    pairs = width // LANES
    chunks = halo.shape[2] // LANES
    n_blocks = 2 * pairs + 1
    kernel = lambda *refs: force_kernel(rows, pairs, chunks, *refs)
    pair_count = rows * pairs * 9 * ATOMS * LANES
    return pl.pallas_call(
        kernel,
        out_shape=jax.ShapeDtypeStruct((3, rows, width), jnp.float32),
        in_specs=[pl.BlockSpec(memory_space=pltpu.VMEM)] * 3,
        out_specs=pl.BlockSpec(memory_space=pltpu.VMEM),
        scratch_shapes=[pltpu.VMEM((3, 3, n_blocks, ATOMS, LANES), jnp.float32)],
        compiler_params=pltpu.CompilerParams(vmem_limit_bytes=48 * 1024 * 1024),
        cost_estimate=pl.CostEstimate(
            flops=20 * pair_count,
            transcendentals=pair_count,
            bytes_accessed=4 * (own.size * 2 + halo.size + flags.size),
        ),
    )(own, halo, flags)


def per_device(positions, velocities, noise, bonds):
    rows_local = positions.shape[2]
    cols_local = positions.shape[3] // ATOMS
    width = cols_local * ATOMS
    coords = positions[0]
    lower_col = passed_along(coords[:, :, width - ATOMS :], "gy", 1)
    upper_col = passed_along(coords[:, :, :ATOMS], "gy", -1)
    widened = jnp.concatenate([lower_col, coords, upper_col], axis=2)
    prev_row = passed_along(widened[:, rows_local - 1 :], "gx", 1)
    next_row = passed_along(widened[:, :1], "gx", -1)
    halo = jnp.concatenate([prev_row, widened, next_row], axis=1)
    chunks = -(-(width + 2 * ATOMS) // LANES)
    halo = jnp.pad(halo, ((0, 0), (0, 0), (0, chunks * LANES - width - 2 * ATOMS)))
    halo = jnp.transpose(halo, (1, 0, 2)) * SCALE
    own = jnp.transpose(coords, (1, 0, 2)) * SCALE
    spread = (lax.broadcasted_iota(jnp.int32, (cols_local, width), 1) // ATOMS
              == lax.broadcasted_iota(jnp.int32, (cols_local, width), 0)).astype(jnp.float32)
    per_cluster = jnp.transpose(bonds.astype(jnp.float32), (0, 2, 1)).reshape(-1, cols_local)
    flags = jnp.dot(per_cluster, spread, precision=lax.Precision.HIGHEST).reshape(rows_local, -1, width)
    force = cluster_forces(own, halo, flags)
    across = ring_shift(force, "rep", 2)
    near = ring_shift(force, "rep", 1)
    far = ring_shift(force, "rep", 3)
    summed_force = (force + across) + (near + far)
    mean_force = summed_force / lax.axis_size("rep")
    new_velocity = friction * velocities + time_step * mean_force[None] + noise_coef * noise
    new_position = positions + time_step * new_velocity
    return (mean_force, new_velocity, new_position)


def solution(mesh):
    in_specs = (
        P("rep", None, "gx", "gy"),
        P("rep", None, "gx", "gy"),
        P("rep", None, "gx", "gy"),
        P("gx", "gy", None),
    )
    out_specs = (P(None, "gx", "gy"), P("rep", None, "gx", "gy"), P("rep", None, "gx", "gy"))
    return jax.shard_map(
        per_device, mesh=mesh, in_specs=in_specs, out_specs=out_specs, check_vma=False
    )
```

```python
import math

import jax
import jax.numpy as jnp
from jax import lax
from jax.experimental import pallas as pl
from jax.experimental.pallas import tpu as pltpu
from jax.sharding import PartitionSpec as P

ATOMS = 64


spacing = 4.0
friction = 0.6
noise_coef = 0.8
time_step = 0.2
offsets_list = ((0, 1), (1, -1), (1, 0), (1, 1), (0, -1), (-1, 1), (-1, 0), (-1, -1))
LANES = 128
SCALE = math.sqrt(0.5 * math.log2(math.e))


def passed_along(value, axis, steps):
    count = lax.axis_size(axis)
    leading, last = (max(0, -steps), min(count, count - steps))
    return lax.ppermute(value, axis, [(source, source + steps) for source in range(leading, last)])


def ring_shift(value, axis, steps):
    count = lax.axis_size(axis)
    return lax.ppermute(value, axis, [(source, (source + steps) % count) for source in range(count)])


def force_kernel(rows, pairs, chunks, own_ref, halo_ref, flag_ref, out_ref, cbuf):
    n_blocks = 2 * pairs + 1
    left = lax.broadcasted_iota(jnp.int32, (ATOMS, LANES), 1) < ATOMS

    def build(h, slot):
        for c in range(3):
            prev = None
            for t in range(chunks):
                if 2 * t - 1 >= n_blocks:
                    break
                r = halo_ref[h, c : c + 1, t * LANES : (t + 1) * LANES]
                tt = jnp.transpose(jnp.broadcast_to(r, (LANES, LANES)))
                if prev is not None and 2 * t - 1 < n_blocks:
                    cbuf[slot, c, 2 * t - 1] = jnp.where(left, prev[ATOMS:], tt[:ATOMS])
                if 2 * t < n_blocks:
                    cbuf[slot, c, 2 * t] = jnp.where(left, tt[:ATOMS], tt[ATOMS:])
                prev = tt

    build(0, 0)
    build(1, 1)

    offsets = ((0, 0),) + offsets_list

    def row_body(i, carry):
        build(i + 2, lax.rem(i + 2, 3))

        def pair_body(k, carry2):
            base = pl.multiple_of(k * LANES, LANES)
            own = own_ref[i, :, pl.ds(base, LANES)]
            flags = flag_ref[i, :, pl.ds(base, LANES)]
            acc = [jnp.zeros((8, LANES), jnp.float32) for _ in range(3)]
            for oi, (dx, dy) in enumerate(offsets):
                slot = lax.rem(i + 1 + dx, 3)
                n = 2 * k + 1 + dy
                if oi == 0:
                    low = jnp.full((8, LANES), -1.0, jnp.float32)
                    high = jnp.full((8, LANES), 5.0, jnp.float32)
                else:
                    f = flags[oi - 1 : oi]
                    low = jnp.broadcast_to((f - 1.0) * 199.0 - 1.0, (8, LANES))
                    high = jnp.broadcast_to((f - 1.0) * 205.0 + 5.0, (8, LANES))
                xs = jnp.broadcast_to(own[0:1] - dx * spacing * SCALE, (8, LANES))
                ys = jnp.broadcast_to(own[1:2] - dy * spacing * SCALE, (8, LANES))
                zs = jnp.broadcast_to(own[2:3], (8, LANES))
                for r in range(ATOMS // 8):
                    cx = cbuf[slot, 0, n, r * 8 : (r + 1) * 8, :]
                    cy = cbuf[slot, 1, n, r * 8 : (r + 1) * 8, :]
                    cz = cbuf[slot, 2, n, r * 8 : (r + 1) * 8, :]
                    ddx = xs - cx
                    ddy = ys - cy
                    ddz = zs - cz
                    t = low - ddx * ddx - ddy * ddy - ddz * ddz
                    w = jnp.exp2(4.0 * t + high) - jnp.exp2(t)
                    acc[0] = acc[0] + w * ddx
                    acc[1] = acc[1] + w * ddy
                    acc[2] = acc[2] + w * ddz
            block = pl.multiple_of((i // 8) * 8, 8)
            mine = lax.broadcasted_iota(jnp.int32, (8, LANES), 0) == i % 8
            for c in range(3):
                row = jnp.sum(acc[c], axis=0, keepdims=True) * (1.0 / SCALE)
                held = out_ref[c, pl.ds(block, 8), pl.ds(base, LANES)]
                out_ref[c, pl.ds(block, 8), pl.ds(base, LANES)] = jnp.where(mine, row, held)
            return carry2

        lax.fori_loop(0, pairs, pair_body, 0)
        return carry

    lax.fori_loop(0, rows, row_body, 0)


def cluster_forces(own, halo, flags):
    rows, _, width = own.shape
    pairs = width // LANES
    chunks = halo.shape[2] // LANES
    n_blocks = 2 * pairs + 1
    kernel = lambda *refs: force_kernel(rows, pairs, chunks, *refs)
    pair_count = rows * pairs * 9 * ATOMS * LANES
    return pl.pallas_call(
        kernel,
        out_shape=jax.ShapeDtypeStruct((3, rows, width), jnp.float32),
        in_specs=[pl.BlockSpec(memory_space=pltpu.VMEM)] * 3,
        out_specs=pl.BlockSpec(memory_space=pltpu.VMEM),
        scratch_shapes=[pltpu.VMEM((3, 3, n_blocks, ATOMS, LANES), jnp.float32)],
        compiler_params=pltpu.CompilerParams(vmem_limit_bytes=48 * 1024 * 1024),
        cost_estimate=pl.CostEstimate(
            flops=20 * pair_count,
            transcendentals=pair_count,
            bytes_accessed=4 * (own.size * 2 + halo.size + flags.size),
        ),
    )(own, halo, flags)


def per_device(positions, velocities, noise, bonds):
    rows_local = positions.shape[2]
    cols_local = positions.shape[3] // ATOMS
    width = cols_local * ATOMS
    coords = positions[0]
    lower_col = passed_along(coords[:, :, width - ATOMS :], "gy", 1)
    upper_col = passed_along(coords[:, :, :ATOMS], "gy", -1)
    widened = jnp.concatenate([lower_col, coords, upper_col], axis=2)
    prev_row = passed_along(widened[:, rows_local - 1 :], "gx", 1)
    next_row = passed_along(widened[:, :1], "gx", -1)
    halo = jnp.concatenate([prev_row, widened, next_row], axis=1)
    chunks = -(-(width + 2 * ATOMS) // LANES)
    halo = jnp.pad(halo, ((0, 0), (0, 0), (0, chunks * LANES - width - 2 * ATOMS)))
    halo = jnp.transpose(halo, (1, 0, 2)) * SCALE
    own = jnp.transpose(coords, (1, 0, 2)) * SCALE
    spread = (lax.broadcasted_iota(jnp.int32, (cols_local, width), 1) // ATOMS
              == lax.broadcasted_iota(jnp.int32, (cols_local, width), 0)).astype(jnp.float32)
    per_cluster = jnp.transpose(bonds.astype(jnp.float32), (0, 2, 1)).reshape(-1, cols_local)
    flags = jnp.dot(per_cluster, spread, precision=lax.Precision.HIGHEST).reshape(rows_local, -1, width)
    force = cluster_forces(own, halo, flags)
    across = ring_shift(force, "rep", 2)
    near = ring_shift(force, "rep", 1)
    far = ring_shift(force, "rep", 3)
    summed_force = (force + across) + (near + far)
    mean_force = summed_force / lax.axis_size("rep")
    new_velocity = friction * velocities + time_step * mean_force[None] + noise_coef * noise
    new_position = positions + time_step * new_velocity
    return (mean_force, new_velocity, new_position)


def solution(mesh):
    in_specs = (
        P("rep", None, "gx", "gy"),
        P("rep", None, "gx", "gy"),
        P("rep", None, "gx", "gy"),
        P("gx", "gy", None),
    )
    out_specs = (P(None, "gx", "gy"), P("rep", None, "gx", "gy"), P("rep", None, "gx", "gy"))
    return jax.shard_map(
        per_device, mesh=mesh, in_specs=in_specs, out_specs=out_specs, check_vma=False
    )
```

```python
import math

import jax
import jax.numpy as jnp
from jax import lax
from jax.experimental import pallas as pl
from jax.experimental.pallas import tpu as pltpu
from jax.sharding import PartitionSpec as P

ATOMS = 64


spacing = 4.0
friction = 0.6
noise_coef = 0.8
time_step = 0.2
offsets_list = ((0, 1), (1, -1), (1, 0), (1, 1), (0, -1), (-1, 1), (-1, 0), (-1, -1))
LANES = 128
SCALE = math.sqrt(0.5 * math.log2(math.e))


def passed_along(value, axis, steps):
    count = lax.axis_size(axis)
    leading, last = (max(0, -steps), min(count, count - steps))
    return lax.ppermute(value, axis, [(source, source + steps) for source in range(leading, last)])


def ring_shift(value, axis, steps):
    count = lax.axis_size(axis)
    return lax.ppermute(value, axis, [(source, (source + steps) % count) for source in range(count)])


def force_kernel(rows, pairs, chunks, own_ref, halo_ref, flag_ref, out_ref, cbuf):
    n_blocks = 2 * pairs + 1
    left = lax.broadcasted_iota(jnp.int32, (ATOMS, LANES), 1) < ATOMS

    def build(h, slot):
        for c in range(3):
            prev = None
            for t in range(chunks):
                if 2 * t - 1 >= n_blocks:
                    break
                r = halo_ref[h, c : c + 1, t * LANES : (t + 1) * LANES]
                tt = jnp.transpose(jnp.broadcast_to(r, (LANES, LANES)))
                if prev is not None and 2 * t - 1 < n_blocks:
                    cbuf[slot, c, 2 * t - 1] = jnp.where(left, prev[ATOMS:], tt[:ATOMS])
                if 2 * t < n_blocks:
                    cbuf[slot, c, 2 * t] = jnp.where(left, tt[:ATOMS], tt[ATOMS:])
                prev = tt

    build(0, 0)
    build(1, 1)

    offsets = ((0, 0),) + offsets_list

    def row_body(i, carry):
        build(i + 2, lax.rem(i + 2, 3))

        def pair_body(k, carry2):
            base = pl.multiple_of(k * LANES, LANES)
            own = own_ref[i, :, pl.ds(base, LANES)]
            flags = flag_ref[i, :, pl.ds(base, LANES)]
            acc = [jnp.zeros((8, LANES), jnp.float32) for _ in range(3)]
            for oi, (dx, dy) in enumerate(offsets):
                slot = lax.rem(i + 1 + dx, 3)
                n = 2 * k + 1 + dy
                if oi == 0:
                    low = jnp.full((8, LANES), -1.0, jnp.float32)
                    high = jnp.full((8, LANES), 5.0, jnp.float32)
                else:
                    f = flags[oi - 1 : oi]
                    low = jnp.broadcast_to((f - 1.0) * 199.0 - 1.0, (8, LANES))
                    high = jnp.broadcast_to((f - 1.0) * 205.0 + 5.0, (8, LANES))
                xs = jnp.broadcast_to(own[0:1] - dx * spacing * SCALE, (8, LANES))
                ys = jnp.broadcast_to(own[1:2] - dy * spacing * SCALE, (8, LANES))
                zs = jnp.broadcast_to(own[2:3], (8, LANES))
                for r in range(ATOMS // 8):
                    cx = cbuf[slot, 0, n, r * 8 : (r + 1) * 8, :]
                    cy = cbuf[slot, 1, n, r * 8 : (r + 1) * 8, :]
                    cz = cbuf[slot, 2, n, r * 8 : (r + 1) * 8, :]
                    ddx = xs - cx
                    ddy = ys - cy
                    ddz = zs - cz
                    t = low - ddx * ddx - ddy * ddy - ddz * ddz
                    w = jnp.exp2(4.0 * t + high) - jnp.exp2(t)
                    acc[0] = acc[0] + w * ddx
                    acc[1] = acc[1] + w * ddy
                    acc[2] = acc[2] + w * ddz
            block = pl.multiple_of((i // 8) * 8, 8)
            mine = lax.broadcasted_iota(jnp.int32, (8, LANES), 0) == i % 8
            for c in range(3):
                row = jnp.sum(acc[c], axis=0, keepdims=True) * (1.0 / SCALE)
                held = out_ref[c, pl.ds(block, 8), pl.ds(base, LANES)]
                out_ref[c, pl.ds(block, 8), pl.ds(base, LANES)] = jnp.where(mine, row, held)
            return carry2

        lax.fori_loop(0, pairs, pair_body, 0)
        return carry

    lax.fori_loop(0, rows, row_body, 0)


def cluster_forces(own, halo, flags):
    rows, _, width = own.shape
    pairs = width // LANES
    chunks = halo.shape[2] // LANES
    n_blocks = 2 * pairs + 1
    kernel = lambda *refs: force_kernel(rows, pairs, chunks, *refs)
    pair_count = rows * pairs * 9 * ATOMS * LANES
    return pl.pallas_call(
        kernel,
        out_shape=jax.ShapeDtypeStruct((3, rows, width), jnp.float32),
        in_specs=[pl.BlockSpec(memory_space=pltpu.VMEM)] * 3,
        out_specs=pl.BlockSpec(memory_space=pltpu.VMEM),
        scratch_shapes=[pltpu.VMEM((3, 3, n_blocks, ATOMS, LANES), jnp.float32)],
        compiler_params=pltpu.CompilerParams(vmem_limit_bytes=48 * 1024 * 1024),
        cost_estimate=pl.CostEstimate(
            flops=20 * pair_count,
            transcendentals=pair_count,
            bytes_accessed=4 * (own.size * 2 + halo.size + flags.size),
        ),
    )(own, halo, flags)


def per_device(positions, velocities, noise, bonds):
    rows_local = positions.shape[2]
    cols_local = positions.shape[3] // ATOMS
    width = cols_local * ATOMS
    coords = positions[0]
    lower_col = passed_along(coords[:, :, width - ATOMS :], "gy", 1)
    upper_col = passed_along(coords[:, :, :ATOMS], "gy", -1)
    widened = jnp.concatenate([lower_col, coords, upper_col], axis=2)
    prev_row = passed_along(widened[:, rows_local - 1 :], "gx", 1)
    next_row = passed_along(widened[:, :1], "gx", -1)
    halo = jnp.concatenate([prev_row, widened, next_row], axis=1)
    chunks = -(-(width + 2 * ATOMS) // LANES)
    halo = jnp.pad(halo, ((0, 0), (0, 0), (0, chunks * LANES - width - 2 * ATOMS)))
    halo = jnp.transpose(halo, (1, 0, 2)) * SCALE
    own = jnp.transpose(coords, (1, 0, 2)) * SCALE
    spread = (lax.broadcasted_iota(jnp.int32, (cols_local, width), 1) // ATOMS
              == lax.broadcasted_iota(jnp.int32, (cols_local, width), 0)).astype(jnp.float32)
    per_cluster = jnp.transpose(bonds.astype(jnp.float32), (0, 2, 1)).reshape(-1, cols_local)
    flags = jnp.dot(per_cluster, spread, precision=lax.Precision.HIGHEST).reshape(rows_local, -1, width)
    half = rows_local // 2
    parts = []
    for start, stop in ((0, half), (half, rows_local)):
        force = cluster_forces(own[start:stop], halo[start : stop + 2], flags[start:stop])
        across = ring_shift(force, "rep", 2)
        near = ring_shift(force, "rep", 1)
        far = ring_shift(force, "rep", 3)
        parts.append((force + across) + (near + far))
    summed_force = jnp.concatenate(parts, axis=1)
    mean_force = summed_force / lax.axis_size("rep")
    new_velocity = friction * velocities + time_step * mean_force[None] + noise_coef * noise
    new_position = positions + time_step * new_velocity
    return (mean_force, new_velocity, new_position)


def solution(mesh):
    in_specs = (
        P("rep", None, "gx", "gy"),
        P("rep", None, "gx", "gy"),
        P("rep", None, "gx", "gy"),
        P("gx", "gy", None),
    )
    out_specs = (P(None, "gx", "gy"), P("rep", None, "gx", "gy"), P("rep", None, "gx", "gy"))
    return jax.shard_map(
        per_device, mesh=mesh, in_specs=in_specs, out_specs=out_specs, check_vma=False
    )
```
